32 devices in a mesh: blk: 8 (over z, y), harvest: 4 (over x, core).
Axes of the slice: x: 2, y: 2, z: 4, core: 2. Of those that a mesh axis runs over, the one named last changes fastest.
Arguments:
- grad_rows: bfloat16 [8192, 8192], P(('blk', 'harvest')), may hold values from -1500 to 1500
- row_weights: float32 [8192], P(('blk', 'harvest')), may hold values from 0.25 to 4
- destinations: int32 [8192, 1], P(('blk', 'harvest')), may hold values from 0 to 7; in each aligned block of 256 rows (0 to 255, 256 to 511, ...) at most 48 rows name the same one
- queries: bfloat16 [128, 8192], P(('blk', 'harvest')), may hold values from -6 to 6
- tile_pattern: int32 [8, 8], replicated, may hold values from 0 to 1, as said below
Outputs:
- scores: bfloat16 [12288, 128], P(('blk', 'harvest'))
The draws below stay inside these ranges and needn't reach their ends.
Inputs may be any that keep to these rules, and one draw needn't show every extreme that they name: `destinations`: in the rows of one device no owner is named more than 48 times, a bound that some block reaches. tile_pattern[a, b] is 1 where the tile of query block a and owner b is scored.
All inputs are finite; a program needn't handle non-finite values.
Results may differ from the reference program's by a relative error of at most 0.0095.
Values may be sent and summed in bfloat16 or wider, within the bound.
No kernel may reach another device: no remote copies, remote signals or barrier semaphores. Data moves between devices by JAX's collectives and lax.ppermute only.
A program may use at most 128 MiB of HBM per device.

```python
import math
import jax
import jax.numpy as jnp
import numpy as np
from jax import lax

K = 8192
R_DEV = 256
CAP = 48
QBLK = 16
Q = 128
ROWS = 8192
SLOTS_ALL = 12288
N_BLK = 8
N_HARVEST = 4
DEVICES = 32


def draw_grad_rows(key, part):
    keys = jax.random.split(key, 3)
    row_place = jnp.arange(ROWS, dtype=jnp.float32)[:, None]
    rising = 1.0 + 2.0 * row_place / max(ROWS - 1, 1)
    row_spread = 10.0 ** jax.random.uniform(keys[1], (ROWS, 1), jnp.float32)
    column_spread = 10.0 ** jax.random.uniform(keys[2], (1, K), jnp.float32)
    base = jnp.clip(jax.random.normal(keys[0], (ROWS, K), jnp.float32), -5.0, 5.0)
    return (base * rising * row_spread * column_spread).astype(jnp.bfloat16)


def draw_tile_pattern(key, part):
    keys = jax.random.split(jax.random.fold_in(key, 7), 2)
    level = jax.random.randint(keys[0], (1, N_BLK), 1, 9)
    rolled = jax.random.randint(keys[1], (N_BLK, N_BLK), 0, 8)
    return (rolled < level).astype(jnp.int32)


def block_levels(own_key, extent, cuts, least, high):
    def one(position, shards_of):
        steps = jax.random.uniform(jax.random.fold_in(jax.random.fold_in(own_key, 6), position), (shards_of,), jnp.float32, least / len(cuts), high / len(cuts))
        return jnp.repeat(jnp.exp(steps), extent[position] // shards_of).reshape((-1,) + (1,) * (len(extent) - position - 1))

    level = one(*cuts[0])
    for cut in cuts[1:]:
        level = level * one(*cut)
    return level


def assign_block(stream_key, own, number, rows, number_of, top, most, lean):
    sequence = jax.random.permutation(stream_key, number_of)
    crowded, usual = shares(number_of, rows * top, most, lean, True), shares(number_of, rows * top, most, lean, False)
    places = jnp.arange(number_of)

    def named(sizes, offset_by):
        used = int((sizes > 0).sum())
        fixed = max(1, used // 4)
        shifted = fixed + (places - fixed + offset_by * (used - fixed)) % max(1, number_of - fixed)
        return jnp.zeros((number_of,), jnp.int32).at[sequence[jnp.where(places < fixed, places, shifted)]].set(jnp.asarray(sizes, jnp.int32))

    sizes = jnp.where(number % 4 == 0, named(crowded, number // 4), named(usual, number - number // 4 - 1))
    mixed = jax.random.permutation(jax.random.fold_in(own, 3), number_of)
    giver, receiver = mixed[0:number_of // 2 * 2:2], mixed[1:number_of // 2 * 2:2]
    slack = jnp.minimum(sizes[giver] - 1, most - sizes[receiver]) // 2
    slack = jnp.where((giver == sequence[0]) | (receiver == sequence[0]) | (sizes[receiver] == 0), 0, jnp.maximum(slack, 0))
    shifted = jax.random.randint(jax.random.fold_in(own, 4), (number_of // 2,), 0, 1 << 20) % (slack + 1)
    sizes = sizes.at[giver].add(-shifted).at[receiver].add(shifted)
    members = jnp.searchsorted(jnp.cumsum(sizes), jnp.arange(rows * top), side="right").astype(jnp.int32)
    listing = members.reshape(top, rows).T
    listing = listing[jax.random.permutation(jax.random.fold_in(own, 1), rows)]
    offset_by = jax.random.randint(jax.random.fold_in(own, 2), (rows, 1), 0, top)
    return jnp.take_along_axis(listing, (jnp.arange(top)[None, :] + offset_by) % top, axis=1)


def shares(count, total, most, slope, full):
    weights = [(1 << 20) // math.isqrt(rank ** slope) + 1 for rank in range(1, count + 1)]
    largest = most if full else min(most, max(-(-total // count), total * weights[0] // sum(weights)))
    least = 1 if total - largest >= count - 1 else 0
    given, rest = [largest] + [least] * (count - 1), total - largest - least * (count - 1)
    while rest > 0:
        free = [i for i in range(1, count) if given[i] < largest] or [i for i in range(1, count) if given[i] < most]
        mass, left = sum([weights[i] for i in free]), rest
        for i in free:
            addition = min(most - given[i], max(1, left * weights[i] // mass), rest)
            given[i] = given[i] + addition
            rest = rest - addition
    return np.array(given)


def noise(stream_key, dims, deviation, bound, cuts=(), held_as=jnp.bfloat16):
    entries = jax.random.normal(stream_key, dims, jnp.float32) * deviation
    if len(cuts) > 0:
        entries = block_levels(stream_key, dims, cuts, -0.22, 0.18) * entries
    return jnp.clip(entries, min=-bound, max=bound).astype(held_as)


def setup_inputs(seed: int = 0) -> dict:
    seeds = jax.random.split(jax.random.key(seed), 6)
    grad_rows = draw_grad_rows(jax.random.fold_in(seeds[5], 71), 0)
    row_weights = jnp.clip(jnp.exp(math.log(4.0) - 2.7725887 * jax.random.uniform(seeds[1], (ROWS,), jnp.float32) ** block_levels(seeds[1], (ROWS,), ((0, 32),), -0.2, 0.2)), 0.25, 4.0)
    destinations_keys = jax.random.split(jax.random.fold_in(seeds[2], 1), ROWS // R_DEV)
    destinations_turns = jax.random.permutation(jax.random.fold_in(seeds[2], 3), ROWS // R_DEV)
    destinations = jax.vmap(lambda own, number: assign_block(jax.random.fold_in(seeds[2], 2), own, number, R_DEV, N_BLK, 1, CAP, 2))(destinations_keys, destinations_turns).reshape((ROWS, 1))
    queries = noise(seeds[3], (Q, K), 1.0, 6.0, ((0, 32),))
    tile_pattern = draw_tile_pattern(jax.random.fold_in(seeds[5], 71), 0)
    return dict(grad_rows=grad_rows, row_weights=row_weights, destinations=destinations, queries=queries, tile_pattern=tile_pattern)


def reference(grad_rows, row_weights, destinations, queries, tile_pattern):
    squares = lax.optimization_barrier(jnp.sum(row_weights[:, None] * jnp.square(grad_rows.astype(jnp.float32)), axis=0))
    total = jnp.sum(row_weights)
    scaling = lax.rsqrt(squares / total + 1e-06)
    prepared = (queries.astype(jnp.float32) * scaling).astype(jnp.bfloat16)
    raw = jnp.dot(grad_rows, prepared.T, preferred_element_type=jnp.float32)
    owner_ids = destinations[:, 0].astype(jnp.int32)
    pattern_rows = tile_pattern.T[owner_ids].astype(jnp.float32)
    full_mask = jnp.repeat(pattern_rows, QBLK, axis=1)
    weight_scale = row_weights * (1.0 / math.sqrt(K))
    value = (raw * weight_scale[:, None] * full_mask).astype(jnp.bfloat16)
    owner_grid = owner_ids.reshape(DEVICES, R_DEV)
    one_hot = (owner_grid[:, :, None] == jnp.arange(N_BLK, dtype=jnp.int32)[None, None, :]).astype(jnp.int32)
    before = jnp.cumsum(one_hot, axis=1) - one_hot
    slot_rank = lax.optimization_barrier(jnp.sum(before * one_hot, axis=2)).astype(jnp.int32)
    source_dev = jnp.arange(DEVICES, dtype=jnp.int32)[:, None]
    source_blk = source_dev // N_HARVEST
    source_harv = source_dev % N_HARVEST
    slot_index = ((owner_grid * N_HARVEST + source_harv) * N_BLK + source_blk) * CAP + slot_rank
    scores = jnp.zeros((SLOTS_ALL, Q), jnp.bfloat16)
    return scores.at[slot_index.reshape(-1).astype(jnp.int32)].set(value)
```

```python
import math

import jax
import jax.numpy as jnp
from jax import lax
from jax.sharding import PartitionSpec as P


def local(grad_rows, row_weights, destinations, queries, tile_pattern):
    blk_count = lax.axis_size("blk")
    harv_count = lax.axis_size("harvest")
    row_count = grad_rows.shape[0]
    width = grad_rows.shape[1]
    capacity = max(3 * row_count // (2 * blk_count), 2)
    block_size = queries.shape[0] * harv_count
    slot_total = blk_count * capacity
    inv_root = 1.0 / math.sqrt(width)

    all_queries = lax.all_gather(queries, ("blk", "harvest"), axis=0, tiled=True)
    query_count = all_queries.shape[0]

    squares = jnp.sum(row_weights[:, None] * jnp.square(grad_rows.astype(jnp.float32)), axis=0)
    total_sq, total_weight = lax.psum((squares, jnp.sum(row_weights)), ("blk", "harvest"))
    scaling = lax.rsqrt(total_sq / total_weight + 1e-06)
    prepared = (all_queries.astype(jnp.float32) * scaling).astype(jnp.bfloat16)

    raw = jnp.einsum("rk,qk->rq", grad_rows, prepared, preferred_element_type=jnp.float32)
    owner_ids = destinations[:, 0]
    pattern_rows = jnp.take(tile_pattern.T, owner_ids, axis=0).astype(jnp.float32)
    full_mask = jnp.repeat(pattern_rows, block_size, axis=1)
    weight_scale = row_weights * inv_root
    value = (raw * weight_scale[:, None] * full_mask).astype(jnp.bfloat16)

    one_hot = (owner_ids[:, None] == jnp.arange(blk_count, dtype=jnp.int32)[None, :]).astype(jnp.int32)
    before = jnp.cumsum(one_hot, axis=0) - one_hot
    slot_rank = jnp.sum(before * one_hot, axis=1)
    slot_index = owner_ids * capacity + slot_rank
    placement = (jnp.arange(slot_total, dtype=jnp.int32)[:, None] == slot_index[None, :]).astype(jnp.bfloat16)
    bucket = jnp.dot(placement, value, preferred_element_type=jnp.float32).astype(jnp.bfloat16)

    received = lax.all_to_all(
        bucket.reshape(blk_count, capacity, query_count), "blk", split_axis=0, concat_axis=0, tiled=True
    )
    return received.reshape(slot_total, query_count)


def solution(mesh):
    in_specs = (
        P(("blk", "harvest"), None),
        P(("blk", "harvest")),
        P(("blk", "harvest"), None),
        P(("blk", "harvest"), None),
        P(),
    )
    out_specs = P(("blk", "harvest"), None)
    return jax.shard_map(local, mesh=mesh, in_specs=in_specs, out_specs=out_specs, check_vma=False)
```

```python
import math

import jax
import jax.numpy as jnp
from jax import lax
from jax.sharding import PartitionSpec as P

AXES = ("blk", "harvest")


def axis_factors(blk_count, harv_count):
    def split(n, lead):
        sizes = []
        if lead and n % 4 == 0:
            sizes.append(4)
            n //= 4
        while n % 2 == 0 and n > 1:
            sizes.append(2)
            n //= 2
        if n > 1:
            sizes.append(n)
        return sizes

    factors = []
    stride = blk_count * harv_count
    for size in split(blk_count, True) + split(harv_count, False):
        stride //= size
        factors.append((size, stride))
    return factors


def coordinate(index, factor):
    size, stride = factor
    return (index // stride) % size


def shifted(factor, shift, device_count):
    size, stride = factor
    return [(i, i + ((coordinate(i, factor) + shift) % size - coordinate(i, factor)) * stride) for i in range(device_count)]


def gather_factor(piece, factor, device_count):
    size, _ = factor
    own = coordinate(lax.axis_index(AXES), factor)
    stacked = jnp.zeros((size,) + piece.shape, piece.dtype)
    stacked = lax.dynamic_update_index_in_dim(stacked, piece, own, 0)
    for shift in range(1, size):
        received = lax.ppermute(piece, AXES, shifted(factor, shift, device_count))
        stacked = lax.dynamic_update_index_in_dim(stacked, received, (own - shift) % size, 0)
    return stacked


def gather_in_order(piece, order, factors, device_count):
    for position in order:
        piece = gather_factor(piece, factors[position], device_count)
    held = list(reversed(order))
    rank = len(factors)
    axes = [held.index(position) for position in range(rank)] + list(range(rank, piece.ndim))
    return jnp.transpose(piece, axes)


def gather_queries(queries, factors, device_count):
    rank = len(factors)
    first, middle, last = [0], list(range(1, rank - 1)), [rank - 1]
    if rank < 3 or queries.shape[0] % 2:
        return gather_in_order(queries, list(range(rank)), factors, device_count).reshape(-1, queries.shape[1])
    first_part = gather_factor(queries, factors[first[0]], device_count)
    half = queries.shape[0] // 2
    halves = []
    for part, order in ((first_part[:, :half], middle), (first_part[:, half:], middle[::-1])):
        gathered = part
        for position in order:
            gathered = gather_factor(gathered, factors[position], device_count)
        held = list(reversed(order))
        axes = [held.index(position) for position in middle] + list(range(len(middle), gathered.ndim))
        halves.append(jnp.transpose(gathered, axes))
    joined = jnp.concatenate(halves, axis=-2)
    joined = jnp.moveaxis(joined, len(middle), 0)
    joined = gather_factor(joined, factors[last[0]], device_count)
    joined = jnp.moveaxis(joined, 0, rank - 1)
    return joined.reshape(-1, queries.shape[1])


def butterfly_sum(values, factors, device_count):
    for factor in factors:
        size, stride = factor
        bit = 1
        while bit < size:
            pairs = [(i, i + ((coordinate(i, factor) ^ bit) - coordinate(i, factor)) * stride) for i in range(device_count)]
            values = values + lax.ppermute(values, AXES, pairs)
            bit *= 2
    return values


def local(grad_rows, row_weights, destinations, queries, tile_pattern):
    blk_count = lax.axis_size("blk")
    harv_count = lax.axis_size("harvest")
    device_count = blk_count * harv_count
    factors = axis_factors(blk_count, harv_count)
    row_count = grad_rows.shape[0]
    width = grad_rows.shape[1]
    capacity = max(3 * row_count // (2 * blk_count), 2)
    block_size = queries.shape[0] * harv_count
    slot_total = blk_count * capacity
    inv_root = 1.0 / math.sqrt(width)

    all_queries = gather_queries(queries, factors, device_count)
    query_count = all_queries.shape[0]

    squares = jnp.sum(row_weights[:, None] * jnp.square(grad_rows.astype(jnp.float32)), axis=0)
    packed = jnp.concatenate([squares, jnp.zeros((128,), jnp.float32).at[0].set(jnp.sum(row_weights))])
    packed = butterfly_sum(packed, factors, device_count)
    total_sq, total_weight = packed[:width], packed[width]
    scaling = lax.rsqrt(total_sq / total_weight + 1e-06)
    prepared = (all_queries.astype(jnp.float32) * scaling).astype(jnp.bfloat16)

    raw = jnp.einsum("rk,qk->rq", grad_rows, prepared, preferred_element_type=jnp.float32)
    owner_ids = destinations[:, 0]
    pattern_rows = jnp.take(tile_pattern.T, owner_ids, axis=0).astype(jnp.float32)
    full_mask = jnp.repeat(pattern_rows, block_size, axis=1)
    weight_scale = row_weights * inv_root
    value = (raw * weight_scale[:, None] * full_mask).astype(jnp.bfloat16)

    one_hot = (owner_ids[:, None] == jnp.arange(blk_count, dtype=jnp.int32)[None, :]).astype(jnp.int32)
    before = jnp.cumsum(one_hot, axis=0) - one_hot
    slot_rank = jnp.sum(before * one_hot, axis=1)
    slot_index = owner_ids * capacity + slot_rank
    placement = (jnp.arange(slot_total, dtype=jnp.int32)[:, None] == slot_index[None, :]).astype(jnp.bfloat16)
    bucket = jnp.dot(placement, value, preferred_element_type=jnp.float32).astype(jnp.bfloat16)

    received = lax.all_to_all(
        bucket.reshape(blk_count, capacity, query_count), "blk", split_axis=0, concat_axis=0, tiled=True
    )
    return received.reshape(slot_total, query_count)


def solution(mesh):
    in_specs = (
        P(AXES, None),
        P(AXES),
        P(AXES, None),
        P(AXES, None),
        P(),
    )
    out_specs = P(AXES, None)
    return jax.shard_map(local, mesh=mesh, in_specs=in_specs, out_specs=out_specs, check_vma=False)
```

```python
import math

import jax
import jax.numpy as jnp
from jax import lax
from jax.sharding import PartitionSpec as P

AXES = ("blk", "harvest")


def axis_factors(blk_count, harv_count):
    def split(n, lead):
        sizes = []
        if lead and n % 4 == 0:
            sizes.append(4)
            n //= 4
        while n % 2 == 0 and n > 1:
            sizes.append(2)
            n //= 2
        if n > 1:
            sizes.append(n)
        return sizes

    factors = []
    stride = blk_count * harv_count
    for size in split(blk_count, True) + split(harv_count, False):
        stride //= size
        factors.append((size, stride))
    return factors


def coordinate(index, factor):
    size, stride = factor
    return (index // stride) % size


def shifted(factor, shift, device_count):
    size, stride = factor
    return [(i, i + ((coordinate(i, factor) + shift) % size - coordinate(i, factor)) * stride) for i in range(device_count)]


def gather_factor(piece, factor, device_count):
    size, _ = factor
    own = coordinate(lax.axis_index(AXES), factor)
    stacked = jnp.zeros((size,) + piece.shape, piece.dtype)
    stacked = lax.dynamic_update_index_in_dim(stacked, piece, own, 0)
    for shift in range(1, size):
        received = lax.ppermute(piece, AXES, shifted(factor, shift, device_count))
        stacked = lax.dynamic_update_index_in_dim(stacked, received, (own - shift) % size, 0)
    return stacked


def gather_rows(piece, factor, device_count):
    rows = piece.shape[0]
    return gather_factor(piece, factor, device_count).reshape((factor[0] * rows,) + piece.shape[1:])


def column_splits(width, parts):
    blocks = width // 128
    sizes = [(blocks // parts + (1 if j < blocks % parts else 0)) * 128 for j in range(parts)]
    starts = [sum(sizes[:j]) for j in range(parts)]
    return list(zip(starts, sizes))


def streamed_scores(grad_rows, queries, scaling, factors, device_count):
    rank = len(factors)
    rows = queries.shape[0]
    first = gather_rows(queries, factors[0], device_count)
    rest = list(range(1, rank))
    streams = max(len(rest), 1)
    raw = None
    for j, (start, size) in enumerate(column_splits(queries.shape[1], streams)):
        order = rest[j:] + rest[:j]
        part = first[:, start:start + size]
        for position in order:
            part = gather_factor(part, factors[position], device_count)
        held = list(reversed(order))
        stacked_rows = part.reshape(-1, size)
        prepared = (stacked_rows.astype(jnp.float32) * scaling[start:start + size]).astype(jnp.bfloat16)
        partial = jnp.einsum(
            "rk,qk->rq", grad_rows[:, start:start + size], prepared, preferred_element_type=jnp.float32
        )
        shape = [factors[p][0] for p in held] + [factors[0][0], rows]
        partial = partial.reshape((grad_rows.shape[0],) + tuple(shape))
        canonical = [held.index(p) + 1 for p in rest]
        lead = len(held) + 1
        partial = jnp.transpose(partial, [0, lead] + canonical + [lead + 1])
        partial = partial.reshape(grad_rows.shape[0], -1)
        raw = partial if raw is None else raw + partial
    return raw


def butterfly_sum(values, factors, device_count):
    for factor in factors:
        size, stride = factor
        bit = 1
        while bit < size:
            pairs = [(i, i + ((coordinate(i, factor) ^ bit) - coordinate(i, factor)) * stride) for i in range(device_count)]
            values = values + lax.ppermute(values, AXES, pairs)
            bit *= 2
    return values


def local(grad_rows, row_weights, destinations, queries, tile_pattern):
    blk_count = lax.axis_size("blk")
    harv_count = lax.axis_size("harvest")
    device_count = blk_count * harv_count
    factors = axis_factors(blk_count, harv_count)
    row_count = grad_rows.shape[0]
    width = grad_rows.shape[1]
    capacity = max(3 * row_count // (2 * blk_count), 2)
    block_size = queries.shape[0] * harv_count
    slot_total = blk_count * capacity
    inv_root = 1.0 / math.sqrt(width)

    query_count = queries.shape[0] * device_count

    squares = jnp.sum(row_weights[:, None] * jnp.square(grad_rows.astype(jnp.float32)), axis=0)
    packed = jnp.concatenate([squares, jnp.zeros((128,), jnp.float32).at[0].set(jnp.sum(row_weights))])
    packed = butterfly_sum(packed, factors, device_count)
    total_sq, total_weight = packed[:width], packed[width]
    scaling = lax.rsqrt(total_sq / total_weight + 1e-06)
    raw = streamed_scores(grad_rows, queries, scaling, factors, device_count)
    owner_ids = destinations[:, 0]
    pattern_rows = jnp.take(tile_pattern.T, owner_ids, axis=0).astype(jnp.float32)
    full_mask = jnp.repeat(pattern_rows, block_size, axis=1)
    weight_scale = row_weights * inv_root
    value = (raw * weight_scale[:, None] * full_mask).astype(jnp.bfloat16)

    one_hot = (owner_ids[:, None] == jnp.arange(blk_count, dtype=jnp.int32)[None, :]).astype(jnp.int32)
    before = jnp.cumsum(one_hot, axis=0) - one_hot
    slot_rank = jnp.sum(before * one_hot, axis=1)
    slot_index = owner_ids * capacity + slot_rank
    placement = (jnp.arange(slot_total, dtype=jnp.int32)[:, None] == slot_index[None, :]).astype(jnp.bfloat16)
    bucket = jnp.dot(placement, value, preferred_element_type=jnp.float32).astype(jnp.bfloat16)

    received = lax.all_to_all(
        bucket.reshape(blk_count, capacity, query_count), "blk", split_axis=0, concat_axis=0, tiled=True
    )
    return received.reshape(slot_total, query_count)


def solution(mesh):
    in_specs = (
        P(AXES, None),
        P(AXES),
        P(AXES, None),
        P(AXES, None),
        P(),
    )
    out_specs = P(AXES, None)
    return jax.shard_map(local, mesh=mesh, in_specs=in_specs, out_specs=out_specs, check_vma=False)
```

```python
import math

import jax
import jax.numpy as jnp
from jax import lax
from jax.sharding import PartitionSpec as P

AXES = ("blk", "harvest")


def axis_factors(blk_count, harv_count):
    def split(n, lead):
        sizes = []
        if lead and n % 4 == 0:
            sizes.append(4)
            n //= 4
        while n % 2 == 0 and n > 1:
            sizes.append(2)
            n //= 2
        if n > 1:
            sizes.append(n)
        return sizes

    factors = []
    stride = blk_count * harv_count
    for size in split(blk_count, True) + split(harv_count, False):
        stride //= size
        factors.append((size, stride))
    return factors


def coordinate(index, factor):
    size, stride = factor
    return (index // stride) % size


def shifted(factor, shift, device_count):
    size, stride = factor
    return [(i, i + ((coordinate(i, factor) + shift) % size - coordinate(i, factor)) * stride) for i in range(device_count)]


def gather_factor(piece, factor, device_count):
    size, _ = factor
    own = coordinate(lax.axis_index(AXES), factor)
    stacked = jnp.zeros((size,) + piece.shape, piece.dtype)
    stacked = lax.dynamic_update_index_in_dim(stacked, piece, own, 0)
    for shift in range(1, size):
        received = lax.ppermute(piece, AXES, shifted(factor, shift, device_count))
        stacked = lax.dynamic_update_index_in_dim(stacked, received, (own - shift) % size, 0)
    return stacked


def gather_rows(piece, factor, device_count):
    rows = piece.shape[0]
    return gather_factor(piece, factor, device_count).reshape((factor[0] * rows,) + piece.shape[1:])


def column_splits(width, parts):
    blocks = width // 128
    sizes = [(blocks // parts + (1 if j < blocks % parts else 0)) * 128 for j in range(parts)]
    starts = [sum(sizes[:j]) for j in range(parts)]
    return list(zip(starts, sizes))


def streamed_scores(grad_rows, queries, scaling, factors, device_count):
    rank = len(factors)
    rows = queries.shape[0]
    row_count = grad_rows.shape[0]
    first = gather_rows(queries, factors[0], device_count)
    if rank == 1:
        prepared = (first.astype(jnp.float32) * scaling).astype(jnp.bfloat16)
        return jnp.einsum("rk,qk->rq", grad_rows, prepared, preferred_element_type=jnp.float32)
    middle = list(range(1, rank - 1))
    last = rank - 1
    splits = column_splits(queries.shape[1], max(len(middle), 1))
    parts, orders = [], []
    for j, (start, size) in enumerate(splits):
        order = middle[j:] + middle[:j]
        part = first[:, start:start + size]
        for position in order:
            part = gather_factor(part, factors[position], device_count)
        parts.append(part.reshape(-1, size))
        orders.append(order)
    joined = jnp.concatenate(parts, axis=1) if len(parts) > 1 else parts[0]

    def partial_scores(block):
        total = None
        for (start, size), order in zip(splits, orders):
            prepared = (block[:, start:start + size].astype(jnp.float32) * scaling[start:start + size]).astype(
                jnp.bfloat16
            )
            partial = jnp.einsum(
                "rk,qk->rq", grad_rows[:, start:start + size], prepared, preferred_element_type=jnp.float32
            )
            held = list(reversed(order))
            shape = [factors[p][0] for p in held] + [factors[0][0], rows]
            partial = partial.reshape((row_count,) + tuple(shape))
            axes = [0, len(held) + 1] + [held.index(p) + 1 for p in middle] + [len(held) + 2]
            partial = jnp.transpose(partial, axes)
            total = partial if total is None else total + partial
        return total

    size_last = factors[last][0]
    own = coordinate(lax.axis_index(AXES), factors[last])
    own_scores = partial_scores(joined)
    stacked = jnp.zeros((size_last,) + own_scores.shape, jnp.float32)
    stacked = lax.dynamic_update_index_in_dim(stacked, own_scores, own, 0)
    for shift in range(1, size_last):
        received = lax.ppermute(joined, AXES, shifted(factors[last], shift, device_count))
        stacked = lax.dynamic_update_index_in_dim(stacked, partial_scores(received), (own - shift) % size_last, 0)
    dims = stacked.ndim
    stacked = jnp.transpose(stacked, [1] + list(range(2, dims - 1)) + [0, dims - 1])
    return stacked.reshape(row_count, -1)


def butterfly_sum(values, factors, device_count):
    for factor in factors:
        size, stride = factor
        bit = 1
        while bit < size:
            pairs = [(i, i + ((coordinate(i, factor) ^ bit) - coordinate(i, factor)) * stride) for i in range(device_count)]
            values = values + lax.ppermute(values, AXES, pairs)
            bit *= 2
    return values


def local(grad_rows, row_weights, destinations, queries, tile_pattern):
    blk_count = lax.axis_size("blk")
    harv_count = lax.axis_size("harvest")
    device_count = blk_count * harv_count
    factors = axis_factors(blk_count, harv_count)
    row_count = grad_rows.shape[0]
    width = grad_rows.shape[1]
    capacity = max(3 * row_count // (2 * blk_count), 2)
    block_size = queries.shape[0] * harv_count
    slot_total = blk_count * capacity
    inv_root = 1.0 / math.sqrt(width)

    query_count = queries.shape[0] * device_count

    squares = jnp.sum(row_weights[:, None] * jnp.square(grad_rows.astype(jnp.float32)), axis=0)
    packed = jnp.concatenate([squares, jnp.zeros((128,), jnp.float32).at[0].set(jnp.sum(row_weights))])
    packed = butterfly_sum(packed, factors, device_count)
    total_sq, total_weight = packed[:width], packed[width]
    scaling = lax.rsqrt(total_sq / total_weight + 1e-06)
    raw = streamed_scores(grad_rows, queries, scaling, factors, device_count)
    owner_ids = destinations[:, 0]
    pattern_rows = jnp.take(tile_pattern.T, owner_ids, axis=0).astype(jnp.float32)
    full_mask = jnp.repeat(pattern_rows, block_size, axis=1)
    weight_scale = row_weights * inv_root
    value = (raw * weight_scale[:, None] * full_mask).astype(jnp.bfloat16)

    one_hot = (owner_ids[:, None] == jnp.arange(blk_count, dtype=jnp.int32)[None, :]).astype(jnp.int32)
    before = jnp.cumsum(one_hot, axis=0) - one_hot
    slot_rank = jnp.sum(before * one_hot, axis=1)
    slot_index = owner_ids * capacity + slot_rank
    placement = (jnp.arange(slot_total, dtype=jnp.int32)[:, None] == slot_index[None, :]).astype(jnp.bfloat16)
    bucket = jnp.dot(placement, value, preferred_element_type=jnp.float32).astype(jnp.bfloat16)

    received = lax.all_to_all(
        bucket.reshape(blk_count, capacity, query_count), "blk", split_axis=0, concat_axis=0, tiled=True
    )
    return received.reshape(slot_total, query_count)


def solution(mesh):
    in_specs = (
        P(AXES, None),
        P(AXES),
        P(AXES, None),
        P(AXES, None),
        P(),
    )
    out_specs = P(AXES, None)
    return jax.shard_map(local, mesh=mesh, in_specs=in_specs, out_specs=out_specs, check_vma=False)
```

```python
import math

import jax
import jax.numpy as jnp
from jax import lax
from jax.sharding import PartitionSpec as P

AXES = ("blk", "harvest")


def axis_factors(blk_count, harv_count):
    def split(n, lead):
        sizes = []
        if lead and n % 4 == 0:
            sizes.append(4)
            n //= 4
        while n % 2 == 0 and n > 1:
            sizes.append(2)
            n //= 2
        if n > 1:
            sizes.append(n)
        return sizes

    factors = []
    stride = blk_count * harv_count
    for size in split(blk_count, True) + split(harv_count, False):
        stride //= size
        factors.append((size, stride))
    return factors


def coordinate(index, factor):
    size, stride = factor
    return (index // stride) % size


def shifted(factor, shift, device_count):
    size, stride = factor
    return [(i, i + ((coordinate(i, factor) + shift) % size - coordinate(i, factor)) * stride) for i in range(device_count)]


def gather_factor(piece, factor, device_count):
    size, _ = factor
    own = coordinate(lax.axis_index(AXES), factor)
    stacked = jnp.zeros((size,) + piece.shape, piece.dtype)
    stacked = lax.dynamic_update_index_in_dim(stacked, piece, own, 0)
    for shift in range(1, size):
        received = lax.ppermute(piece, AXES, shifted(factor, shift, device_count))
        stacked = lax.dynamic_update_index_in_dim(stacked, received, (own - shift) % size, 0)
    return stacked


def gather_rows(piece, factor, device_count):
    rows = piece.shape[0]
    return gather_factor(piece, factor, device_count).reshape((factor[0] * rows,) + piece.shape[1:])


def column_splits(width, parts):
    blocks = width // 128
    sizes = [(blocks // parts + (1 if j < blocks % parts else 0)) * 128 for j in range(parts)]
    starts = [sum(sizes[:j]) for j in range(parts)]
    return list(zip(starts, sizes))


def streamed_scores(grad_rows, queries, scaling, factors, device_count, first):
    rank = len(factors)
    rows = queries.shape[0]
    row_count = grad_rows.shape[0]
    if rank == 1:
        prepared = (first.astype(jnp.float32) * scaling).astype(jnp.bfloat16)
        return jnp.einsum("rk,qk->rq", grad_rows, prepared, preferred_element_type=jnp.float32)
    middle = list(range(1, rank - 1))
    last = rank - 1
    splits = column_splits(queries.shape[1], max(len(middle), 1))
    parts, orders = [], []
    for j, (start, size) in enumerate(splits):
        order = middle[j:] + middle[:j]
        part = first[:, start:start + size]
        for position in order:
            part = gather_factor(part, factors[position], device_count)
        parts.append(part.reshape(-1, size))
        orders.append(order)
    joined = jnp.concatenate(parts, axis=1) if len(parts) > 1 else parts[0]

    def partial_scores(block):
        total = None
        for (start, size), order in zip(splits, orders):
            prepared = (block[:, start:start + size].astype(jnp.float32) * scaling[start:start + size]).astype(
                jnp.bfloat16
            )
            partial = jnp.einsum(
                "rk,qk->rq", grad_rows[:, start:start + size], prepared, preferred_element_type=jnp.float32
            )
            held = list(reversed(order))
            shape = [factors[p][0] for p in held] + [factors[0][0], rows]
            partial = partial.reshape((row_count,) + tuple(shape))
            axes = [0, len(held) + 1] + [held.index(p) + 1 for p in middle] + [len(held) + 2]
            partial = jnp.transpose(partial, axes)
            total = partial if total is None else total + partial
        return total

    size_last = factors[last][0]
    own = coordinate(lax.axis_index(AXES), factors[last])
    own_scores = partial_scores(joined)
    stacked = jnp.zeros((size_last,) + own_scores.shape, jnp.float32)
    stacked = lax.dynamic_update_index_in_dim(stacked, own_scores, own, 0)
    for shift in range(1, size_last):
        received = lax.ppermute(joined, AXES, shifted(factors[last], shift, device_count))
        stacked = lax.dynamic_update_index_in_dim(stacked, partial_scores(received), (own - shift) % size_last, 0)
    dims = stacked.ndim
    stacked = jnp.transpose(stacked, [1] + list(range(2, dims - 1)) + [0, dims - 1])
    return stacked.reshape(row_count, -1)


def butterfly_sum(values, factors, device_count):
    for factor in factors:
        size, stride = factor
        bit = 1
        while bit < size:
            pairs = [(i, i + ((coordinate(i, factor) ^ bit) - coordinate(i, factor)) * stride) for i in range(device_count)]
            values = values + lax.ppermute(values, AXES, pairs)
            bit *= 2
    return values


def local(grad_rows, row_weights, destinations, queries, tile_pattern):
    blk_count = lax.axis_size("blk")
    harv_count = lax.axis_size("harvest")
    device_count = blk_count * harv_count
    factors = axis_factors(blk_count, harv_count)
    row_count = grad_rows.shape[0]
    width = grad_rows.shape[1]
    capacity = max(3 * row_count // (2 * blk_count), 2)
    block_size = queries.shape[0] * harv_count
    slot_total = blk_count * capacity
    inv_root = 1.0 / math.sqrt(width)

    query_count = queries.shape[0] * device_count

    squares = jnp.sum(row_weights[:, None] * jnp.square(grad_rows.astype(jnp.float32)), axis=0)
    packed = jnp.concatenate([squares, jnp.zeros((128,), jnp.float32).at[0].set(jnp.sum(row_weights))])
    first = gather_rows(queries, factors[0], device_count)
    first, packed = lax.optimization_barrier((first, packed))
    packed = butterfly_sum(packed, factors, device_count)
    total_sq, total_weight = packed[:width], packed[width]
    scaling = lax.rsqrt(total_sq / total_weight + 1e-06)
    raw = streamed_scores(grad_rows, queries, scaling, factors, device_count, first)
    owner_ids = destinations[:, 0]
    pattern_rows = jnp.take(tile_pattern.T, owner_ids, axis=0).astype(jnp.float32)
    full_mask = jnp.repeat(pattern_rows, block_size, axis=1)
    weight_scale = row_weights * inv_root
    value = (raw * weight_scale[:, None] * full_mask).astype(jnp.bfloat16)

    one_hot = (owner_ids[:, None] == jnp.arange(blk_count, dtype=jnp.int32)[None, :]).astype(jnp.int32)
    before = jnp.cumsum(one_hot, axis=0) - one_hot
    slot_rank = jnp.sum(before * one_hot, axis=1)
    slot_index = owner_ids * capacity + slot_rank
    placement = (jnp.arange(slot_total, dtype=jnp.int32)[:, None] == slot_index[None, :]).astype(jnp.bfloat16)
    bucket = jnp.dot(placement, value, preferred_element_type=jnp.float32).astype(jnp.bfloat16)

    received = lax.all_to_all(
        bucket.reshape(blk_count, capacity, query_count), "blk", split_axis=0, concat_axis=0, tiled=True
    )
    return received.reshape(slot_total, query_count)


def solution(mesh):
    in_specs = (
        P(AXES, None),
        P(AXES),
        P(AXES, None),
        P(AXES, None),
        P(),
    )
    out_specs = P(AXES, None)
    return jax.shard_map(local, mesh=mesh, in_specs=in_specs, out_specs=out_specs, check_vma=False)
```

```python
import math

import jax
import jax.numpy as jnp
from jax import lax
from jax.sharding import PartitionSpec as P

AXES = ("blk", "harvest")


def axis_factors(blk_count, harv_count):
    def split(n, lead):
        sizes = []
        if lead and n % 4 == 0:
            sizes.append(4)
            n //= 4
        while n % 2 == 0 and n > 1:
            sizes.append(2)
            n //= 2
        if n > 1:
            sizes.append(n)
        return sizes

    factors = []
    stride = blk_count * harv_count
    for size in split(blk_count, True) + split(harv_count, False):
        stride //= size
        factors.append((size, stride))
    return factors


def coordinate(index, factor):
    size, stride = factor
    return (index // stride) % size


def shifted(factor, shift, device_count):
    size, stride = factor
    return [(i, i + ((coordinate(i, factor) + shift) % size - coordinate(i, factor)) * stride) for i in range(device_count)]


def gather_factor(piece, factor, device_count):
    size, _ = factor
    own = coordinate(lax.axis_index(AXES), factor)
    stacked = jnp.zeros((size,) + piece.shape, piece.dtype)
    stacked = lax.dynamic_update_index_in_dim(stacked, piece, own, 0)
    for shift in range(1, size):
        received = lax.ppermute(piece, AXES, shifted(factor, shift, device_count))
        stacked = lax.dynamic_update_index_in_dim(stacked, received, (own - shift) % size, 0)
    return stacked


def gather_rows(piece, factor, device_count):
    rows = piece.shape[0]
    return gather_factor(piece, factor, device_count).reshape((factor[0] * rows,) + piece.shape[1:])


def column_splits(width, parts):
    blocks = width // 128
    sizes = [(blocks // parts + (1 if j < blocks % parts else 0)) * 128 for j in range(parts)]
    starts = [sum(sizes[:j]) for j in range(parts)]
    return list(zip(starts, sizes))


def streamed_scores(grad_rows, queries, scaling, factors, device_count, first):
    rank = len(factors)
    rows = queries.shape[0]
    row_count = grad_rows.shape[0]
    if rank == 1:
        prepared = (first.astype(jnp.float32) * scaling).astype(jnp.bfloat16)
        return jnp.einsum("rk,qk->rq", grad_rows, prepared, preferred_element_type=jnp.float32)
    middle = list(range(1, rank - 1))
    last = rank - 1
    splits = column_splits(queries.shape[1], max(len(middle), 1))
    parts, orders = [], []
    for j, (start, size) in enumerate(splits):
        order = middle[j:] + middle[:j]
        part = first[:, start:start + size]
        for position in order:
            part = gather_factor(part, factors[position], device_count)
        parts.append(part.reshape(-1, size))
        orders.append(order)
    joined = jnp.concatenate(parts, axis=1) if len(parts) > 1 else parts[0]

    def partial_scores(block):
        total = None
        for (start, size), order in zip(splits, orders):
            prepared = (block[:, start:start + size].astype(jnp.float32) * scaling[start:start + size]).astype(
                jnp.bfloat16
            )
            partial = jnp.einsum(
                "rk,qk->rq", grad_rows[:, start:start + size], prepared, preferred_element_type=jnp.float32
            )
            held = list(reversed(order))
            shape = [factors[p][0] for p in held] + [factors[0][0], rows]
            partial = partial.reshape((row_count,) + tuple(shape))
            axes = [0, len(held) + 1] + [held.index(p) + 1 for p in middle] + [len(held) + 2]
            partial = jnp.transpose(partial, axes)
            total = partial if total is None else total + partial
        return total

    size_last = factors[last][0]
    own = coordinate(lax.axis_index(AXES), factors[last])
    own_scores = partial_scores(joined)
    stacked = jnp.zeros((size_last,) + own_scores.shape, jnp.float32)
    stacked = lax.dynamic_update_index_in_dim(stacked, own_scores, own, 0)
    for shift in range(1, size_last):
        received = lax.ppermute(joined, AXES, shifted(factors[last], shift, device_count))
        stacked = lax.dynamic_update_index_in_dim(stacked, partial_scores(received), (own - shift) % size_last, 0)
    dims = stacked.ndim
    stacked = jnp.transpose(stacked, [1] + list(range(2, dims - 1)) + [0, dims - 1])
    return stacked.reshape(row_count, -1)


def butterfly_sum(values, factors, device_count):
    for factor in factors[-1:] + factors[:-1]:
        size, stride = factor
        bit = 1
        while bit < size:
            pairs = [(i, i + ((coordinate(i, factor) ^ bit) - coordinate(i, factor)) * stride) for i in range(device_count)]
            values = values + lax.ppermute(values, AXES, pairs)
            bit *= 2
    return values


def local(grad_rows, row_weights, destinations, queries, tile_pattern):
    blk_count = lax.axis_size("blk")
    harv_count = lax.axis_size("harvest")
    device_count = blk_count * harv_count
    factors = axis_factors(blk_count, harv_count)
    row_count = grad_rows.shape[0]
    width = grad_rows.shape[1]
    capacity = max(3 * row_count // (2 * blk_count), 2)
    block_size = queries.shape[0] * harv_count
    slot_total = blk_count * capacity
    inv_root = 1.0 / math.sqrt(width)

    query_count = queries.shape[0] * device_count

    squares = jnp.sum(row_weights[:, None] * jnp.square(grad_rows.astype(jnp.float32)), axis=0)
    packed = jnp.concatenate([squares, jnp.zeros((128,), jnp.float32).at[0].set(jnp.sum(row_weights))])
    first = gather_rows(queries, factors[0], device_count)
    first, packed = lax.optimization_barrier((first, packed))
    packed = butterfly_sum(packed, factors, device_count)
    total_sq, total_weight = packed[:width], packed[width]
    scaling = lax.rsqrt(total_sq / total_weight + 1e-06)
    raw = streamed_scores(grad_rows, queries, scaling, factors, device_count, first)
    owner_ids = destinations[:, 0]
    pattern_rows = jnp.take(tile_pattern.T, owner_ids, axis=0).astype(jnp.float32)
    full_mask = jnp.repeat(pattern_rows, block_size, axis=1)
    weight_scale = row_weights * inv_root
    value = (raw * weight_scale[:, None] * full_mask).astype(jnp.bfloat16)

    one_hot = (owner_ids[:, None] == jnp.arange(blk_count, dtype=jnp.int32)[None, :]).astype(jnp.int32)
    before = jnp.cumsum(one_hot, axis=0) - one_hot
    slot_rank = jnp.sum(before * one_hot, axis=1)
    slot_index = owner_ids * capacity + slot_rank
    placement = (jnp.arange(slot_total, dtype=jnp.int32)[:, None] == slot_index[None, :]).astype(jnp.bfloat16)
    bucket = jnp.dot(placement, value, preferred_element_type=jnp.float32).astype(jnp.bfloat16)

    received = lax.all_to_all(
        bucket.reshape(blk_count, capacity, query_count), "blk", split_axis=0, concat_axis=0, tiled=True
    )
    return received.reshape(slot_total, query_count)


def solution(mesh):
    in_specs = (
        P(AXES, None),
        P(AXES),
        P(AXES, None),
        P(AXES, None),
        P(),
    )
    out_specs = P(AXES, None)
    return jax.shard_map(local, mesh=mesh, in_specs=in_specs, out_specs=out_specs, check_vma=False)
```

```python
import math

import jax
import jax.numpy as jnp
from jax import lax
from jax.sharding import PartitionSpec as P

AXES = ("blk", "harvest")


def axis_factors(blk_count, harv_count):
    def split(n, lead):
        sizes = []
        if lead and n % 4 == 0:
            sizes.append(4)
            n //= 4
        while n % 2 == 0 and n > 1:
            sizes.append(2)
            n //= 2
        if n > 1:
            sizes.append(n)
        return sizes

    factors = []
    stride = blk_count * harv_count
    for size in split(blk_count, True) + split(harv_count, False):
        stride //= size
        factors.append((size, stride))
    return factors


def coordinate(index, factor):
    size, stride = factor
    return (index // stride) % size


def shifted(factor, shift, device_count):
    size, stride = factor
    return [(i, i + ((coordinate(i, factor) + shift) % size - coordinate(i, factor)) * stride) for i in range(device_count)]


def gather_factor(piece, factor, device_count):
    size, _ = factor
    own = coordinate(lax.axis_index(AXES), factor)
    stacked = jnp.zeros((size,) + piece.shape, piece.dtype)
    stacked = lax.dynamic_update_index_in_dim(stacked, piece, own, 0)
    for shift in range(1, size):
        received = lax.ppermute(piece, AXES, shifted(factor, shift, device_count))
        stacked = lax.dynamic_update_index_in_dim(stacked, received, (own - shift) % size, 0)
    return stacked


def gather_rows(piece, factor, device_count):
    rows = piece.shape[0]
    return gather_factor(piece, factor, device_count).reshape((factor[0] * rows,) + piece.shape[1:])


def column_splits(width, parts):
    blocks = width // 128
    sizes = [(blocks // parts + (1 if j < blocks % parts else 0)) * 128 for j in range(parts)]
    starts = [sum(sizes[:j]) for j in range(parts)]
    return list(zip(starts, sizes))


def gather_streams(first, factors, device_count):
    rank = len(factors)
    middle = list(range(1, rank - 1))
    splits = column_splits(first.shape[1], max(len(middle), 1))
    parts, orders = [], []
    for j, (start, size) in enumerate(splits):
        order = middle[j:] + middle[:j]
        part = first[:, start:start + size]
        for position in order:
            part = gather_factor(part, factors[position], device_count)
        parts.append(part.reshape(-1, size))
        orders.append(order)
    joined = jnp.concatenate(parts, axis=1) if len(parts) > 1 else parts[0]
    return joined, splits, orders


def exchange_and_score(grad_rows, joined, scaling, splits, orders, factors, rows, device_count):
    rank = len(factors)
    middle = list(range(1, rank - 1))
    last = rank - 1
    row_count = grad_rows.shape[0]
    size_last = factors[last][0]
    own = coordinate(lax.axis_index(AXES), factors[last])
    blocks = [joined] + [
        lax.ppermute(joined, AXES, shifted(factors[last], shift, device_count)) for shift in range(1, size_last)
    ]
    full = jnp.concatenate(blocks, axis=0) if size_last > 1 else joined
    total = None
    for (start, size), order in zip(splits, orders):
        prepared = (full[:, start:start + size].astype(jnp.float32) * scaling[start:start + size]).astype(jnp.bfloat16)
        partial = jnp.einsum(
            "rk,qk->rq", grad_rows[:, start:start + size], prepared, preferred_element_type=jnp.float32
        )
        held = list(reversed(order))
        shape = [size_last] + [factors[p][0] for p in held] + [factors[0][0], rows]
        partial = partial.reshape((row_count,) + tuple(shape))
        axes = [0, 1, len(held) + 2] + [held.index(p) + 2 for p in middle] + [len(held) + 3]
        partial = jnp.transpose(partial, axes)
        total = partial if total is None else total + partial
    reverse = jnp.flip(total, axis=1)
    doubled = jnp.concatenate([reverse, reverse], axis=1)
    ordered = lax.dynamic_slice_in_dim(doubled, size_last - 1 - own, size_last, axis=1)
    dims = ordered.ndim
    ordered = jnp.transpose(ordered, [0] + list(range(2, dims - 1)) + [1, dims - 1])
    return ordered.reshape(row_count, -1)


def butterfly_sum(values, factors, device_count):
    for factor in factors:
        size, stride = factor
        bit = 1
        while bit < size:
            pairs = [(i, i + ((coordinate(i, factor) ^ bit) - coordinate(i, factor)) * stride) for i in range(device_count)]
            values = values + lax.ppermute(values, AXES, pairs)
            bit *= 2
    return values


def local(grad_rows, row_weights, destinations, queries, tile_pattern):
    blk_count = lax.axis_size("blk")
    harv_count = lax.axis_size("harvest")
    device_count = blk_count * harv_count
    factors = axis_factors(blk_count, harv_count)
    row_count = grad_rows.shape[0]
    width = grad_rows.shape[1]
    capacity = max(3 * row_count // (2 * blk_count), 2)
    block_size = queries.shape[0] * harv_count
    slot_total = blk_count * capacity
    inv_root = 1.0 / math.sqrt(width)

    query_count = queries.shape[0] * device_count

    squares = jnp.sum(row_weights[:, None] * jnp.square(grad_rows.astype(jnp.float32)), axis=0)
    packed = jnp.concatenate([squares, jnp.zeros((128,), jnp.float32).at[0].set(jnp.sum(row_weights))])
    first = gather_rows(queries, factors[0], device_count)
    first, packed = lax.optimization_barrier((first, packed))
    levels = factors[-1:] + factors[:-1]
    packed = butterfly_sum(packed, levels[:-1], device_count)
    joined, splits, orders = gather_streams(first, factors, device_count)
    joined, packed = lax.optimization_barrier((joined, packed))
    packed = butterfly_sum(packed, levels[-1:], device_count)
    total_sq, total_weight = packed[:width], packed[width]
    scaling = lax.rsqrt(total_sq / total_weight + 1e-06)
    raw = exchange_and_score(grad_rows, joined, scaling, splits, orders, factors, queries.shape[0], device_count)
    owner_ids = destinations[:, 0]
    pattern_rows = jnp.take(tile_pattern.T, owner_ids, axis=0).astype(jnp.float32)
    full_mask = jnp.repeat(pattern_rows, block_size, axis=1)
    weight_scale = row_weights * inv_root
    value = (raw * weight_scale[:, None] * full_mask).astype(jnp.bfloat16)

    one_hot = (owner_ids[:, None] == jnp.arange(blk_count, dtype=jnp.int32)[None, :]).astype(jnp.int32)
    before = jnp.cumsum(one_hot, axis=0) - one_hot
    slot_rank = jnp.sum(before * one_hot, axis=1)
    slot_index = owner_ids * capacity + slot_rank
    placement = (jnp.arange(slot_total, dtype=jnp.int32)[:, None] == slot_index[None, :]).astype(jnp.bfloat16)
    bucket = jnp.dot(placement, value, preferred_element_type=jnp.float32).astype(jnp.bfloat16)

    received = lax.all_to_all(
        bucket.reshape(blk_count, capacity, query_count), "blk", split_axis=0, concat_axis=0, tiled=True
    )
    return received.reshape(slot_total, query_count)


def solution(mesh):
    in_specs = (
        P(AXES, None),
        P(AXES),
        P(AXES, None),
        P(AXES, None),
        P(),
    )
    out_specs = P(AXES, None)
    return jax.shard_map(local, mesh=mesh, in_specs=in_specs, out_specs=out_specs, check_vma=False)
```

```python
import math

import jax
import jax.numpy as jnp
from jax import lax
from jax.sharding import PartitionSpec as P

AXES = ("blk", "harvest")


def axis_factors(blk_count, harv_count):
    def split(n, lead):
        sizes = []
        if lead and n % 4 == 0:
            sizes.append(4)
            n //= 4
        while n % 2 == 0 and n > 1:
            sizes.append(2)
            n //= 2
        if n > 1:
            sizes.append(n)
        return sizes

    factors = []
    stride = blk_count * harv_count
    for size in split(blk_count, True) + split(harv_count, False):
        stride //= size
        factors.append((size, stride))
    return factors


def coordinate(index, factor):
    size, stride = factor
    return (index // stride) % size


def shifted(factor, shift, device_count):
    size, stride = factor
    return [(i, i + ((coordinate(i, factor) + shift) % size - coordinate(i, factor)) * stride) for i in range(device_count)]


def gather_factor(piece, factor, device_count):
    size, _ = factor
    own = coordinate(lax.axis_index(AXES), factor)
    stacked = jnp.zeros((size,) + piece.shape, piece.dtype)
    stacked = lax.dynamic_update_index_in_dim(stacked, piece, own, 0)
    for shift in range(1, size):
        received = lax.ppermute(piece, AXES, shifted(factor, shift, device_count))
        stacked = lax.dynamic_update_index_in_dim(stacked, received, (own - shift) % size, 0)
    return stacked


def gather_rows(piece, factor, device_count):
    rows = piece.shape[0]
    return gather_factor(piece, factor, device_count).reshape((factor[0] * rows,) + piece.shape[1:])


def column_splits(width, parts):
    blocks = width // 128
    sizes = [(blocks // parts + (1 if j < blocks % parts else 0)) * 128 for j in range(parts)]
    starts = [sum(sizes[:j]) for j in range(parts)]
    return list(zip(starts, sizes))


def gather_streams(first, factors, device_count):
    rank = len(factors)
    middle = list(range(1, rank - 1))
    splits = column_splits(first.shape[1], max(len(middle), 1))
    parts, orders = [], []
    for j, (start, size) in enumerate(splits):
        order = middle[j:] + middle[:j]
        part = first[:, start:start + size]
        for position in order:
            part = gather_factor(part, factors[position], device_count)
        parts.append(part.reshape(-1, size))
        orders.append(order)
    joined = jnp.concatenate(parts, axis=1) if len(parts) > 1 else parts[0]
    return joined, splits, orders


def exchange_and_score(grad_rows, joined, scaling, splits, orders, factors, rows, device_count):
    rank = len(factors)
    middle = list(range(1, rank - 1))
    last = rank - 1
    row_count = grad_rows.shape[0]
    size_last = factors[last][0]
    own = coordinate(lax.axis_index(AXES), factors[last])
    blocks = [joined] + [
        lax.ppermute(joined, AXES, shifted(factors[last], shift, device_count)) for shift in range(1, size_last)
    ]
    full = jnp.concatenate(blocks, axis=0) if size_last > 1 else joined
    total = None
    for (start, size), order in zip(splits, orders):
        prepared = (full[:, start:start + size].astype(jnp.float32) * scaling[start:start + size]).astype(jnp.bfloat16)
        partial = jnp.einsum(
            "rk,qk->rq", grad_rows[:, start:start + size], prepared, preferred_element_type=jnp.float32
        )
        held = list(reversed(order))
        shape = [size_last] + [factors[p][0] for p in held] + [factors[0][0], rows]
        partial = partial.reshape((row_count,) + tuple(shape))
        axes = [0, 1, len(held) + 2] + [held.index(p) + 2 for p in middle] + [len(held) + 3]
        partial = jnp.transpose(partial, axes)
        total = partial if total is None else total + partial
    reverse = jnp.flip(total, axis=1)
    doubled = jnp.concatenate([reverse, reverse], axis=1)
    ordered = lax.dynamic_slice_in_dim(doubled, size_last - 1 - own, size_last, axis=1)
    dims = ordered.ndim
    ordered = jnp.transpose(ordered, [0] + list(range(2, dims - 1)) + [1, dims - 1])
    return ordered.reshape(row_count, -1)


def butterfly_sum(values, factors, device_count):
    for factor in factors:
        size, stride = factor
        bit = 1
        while bit < size:
            pairs = [(i, i + ((coordinate(i, factor) ^ bit) - coordinate(i, factor)) * stride) for i in range(device_count)]
            values = values + lax.ppermute(values, AXES, pairs)
            bit *= 2
    return values


def local(grad_rows, row_weights, destinations, queries, tile_pattern):
    blk_count = lax.axis_size("blk")
    harv_count = lax.axis_size("harvest")
    device_count = blk_count * harv_count
    factors = axis_factors(blk_count, harv_count)
    row_count = grad_rows.shape[0]
    width = grad_rows.shape[1]
    capacity = max(3 * row_count // (2 * blk_count), 2)
    block_size = queries.shape[0] * harv_count
    slot_total = blk_count * capacity
    inv_root = 1.0 / math.sqrt(width)

    query_count = queries.shape[0] * device_count

    squares = jnp.sum(row_weights[:, None] * jnp.square(grad_rows.astype(jnp.float32)), axis=0)
    packed = jnp.concatenate([squares, jnp.zeros((128,), jnp.float32).at[0].set(jnp.sum(row_weights))])
    first = gather_rows(queries, factors[0], device_count)
    first, packed, destinations, tile_pattern = lax.optimization_barrier((first, packed, destinations, tile_pattern))
    levels = list(factors)
    packed = butterfly_sum(packed, levels[:-1], device_count)
    joined, splits, orders = gather_streams(first, factors, device_count)
    joined, packed = lax.optimization_barrier((joined, packed))
    packed = butterfly_sum(packed, levels[-1:], device_count)
    total_sq, total_weight = packed[:width], packed[width]
    scaling = lax.rsqrt(total_sq / total_weight + 1e-06)
    raw = exchange_and_score(grad_rows, joined, scaling, splits, orders, factors, queries.shape[0], device_count)
    owner_ids = destinations[:, 0]
    pattern_rows = jnp.take(tile_pattern.T, owner_ids, axis=0).astype(jnp.float32)
    full_mask = jnp.repeat(pattern_rows, block_size, axis=1)
    weight_scale = row_weights * inv_root
    value = (raw * weight_scale[:, None] * full_mask).astype(jnp.bfloat16)

    one_hot = (owner_ids[:, None] == jnp.arange(blk_count, dtype=jnp.int32)[None, :]).astype(jnp.int32)
    before = jnp.cumsum(one_hot, axis=0) - one_hot
    slot_rank = jnp.sum(before * one_hot, axis=1)
    slot_index = owner_ids * capacity + slot_rank
    placement = (jnp.arange(slot_total, dtype=jnp.int32)[:, None] == slot_index[None, :]).astype(jnp.bfloat16)
    bucket = jnp.dot(placement, value, preferred_element_type=jnp.float32).astype(jnp.bfloat16)

    received = lax.all_to_all(
        bucket.reshape(blk_count, capacity, query_count), "blk", split_axis=0, concat_axis=0, tiled=True
    )
    return received.reshape(slot_total, query_count)


def solution(mesh):
    in_specs = (
        P(AXES, None),
        P(AXES),
        P(AXES, None),
        P(AXES, None),
        P(),
    )
    out_specs = P(AXES, None)
    return jax.shard_map(local, mesh=mesh, in_specs=in_specs, out_specs=out_specs, check_vma=False)
```

```python
import math

import jax
import jax.numpy as jnp
from jax import lax
from jax.sharding import PartitionSpec as P

AXES = ("blk", "harvest")


def axis_factors(blk_count, harv_count):
    def split(n, lead):
        sizes = []
        if lead and n % 4 == 0:
            sizes.append(4)
            n //= 4
        while n % 2 == 0 and n > 1:
            sizes.append(2)
            n //= 2
        if n > 1:
            sizes.append(n)
        return sizes

    factors = []
    stride = blk_count * harv_count
    for size in split(blk_count, True) + split(harv_count, False):
        stride //= size
        factors.append((size, stride))
    return factors


def coordinate(index, factor):
    size, stride = factor
    return (index // stride) % size


def shifted(factor, shift, device_count):
    size, stride = factor
    return [(i, i + ((coordinate(i, factor) + shift) % size - coordinate(i, factor)) * stride) for i in range(device_count)]


def gather_factor(piece, factor, device_count):
    size, _ = factor
    own = coordinate(lax.axis_index(AXES), factor)
    stacked = jnp.zeros((size,) + piece.shape, piece.dtype)
    stacked = lax.dynamic_update_index_in_dim(stacked, piece, own, 0)
    for shift in range(1, size):
        received = lax.ppermute(piece, AXES, shifted(factor, shift, device_count))
        stacked = lax.dynamic_update_index_in_dim(stacked, received, (own - shift) % size, 0)
    return stacked


def gather_rows(piece, factor, device_count):
    rows = piece.shape[0]
    return gather_factor(piece, factor, device_count).reshape((factor[0] * rows,) + piece.shape[1:])


def column_splits(width, parts):
    blocks = width // 128
    sizes = [(blocks // parts + (1 if j < blocks % parts else 0)) * 128 for j in range(parts)]
    starts = [sum(sizes[:j]) for j in range(parts)]
    return list(zip(starts, sizes))


def psum_steps(factors):
    steps = []
    for factor in factors:
        bit = 1
        while bit < factor[0]:
            steps.append((factor, bit))
            bit *= 2
    return steps


def psum_step(values, step, device_count):
    factor, bit = step
    size, stride = factor
    pairs = [(i, i + ((coordinate(i, factor) ^ bit) - coordinate(i, factor)) * stride) for i in range(device_count)]
    return values + lax.ppermute(values, AXES, pairs)


def gather_streams(first, packed, steps, factors, device_count):
    rank = len(factors)
    middle = list(range(1, rank - 1))
    splits = column_splits(first.shape[1], max(len(middle), 1))
    orders = [middle[j:] + middle[:j] for j in range(len(splits))]
    parts = [first[:, start:start + size] for start, size in splits]
    done = 0
    for level in range(len(middle)):
        parts = [gather_factor(part, factors[order[level]], device_count) for part, order in zip(parts, orders)]
        target = min(level + 2, len(steps) - 1) if level + 1 < len(middle) else len(steps) - 1
        while done < target:
            packed = psum_step(packed, steps[done], device_count)
            done += 1
        parts, packed = lax.optimization_barrier((parts, packed))
    while done < len(steps):
        packed = psum_step(packed, steps[done], device_count)
        done += 1
    parts = [part.reshape(-1, size) for part, (start, size) in zip(parts, splits)]
    joined = jnp.concatenate(parts, axis=1) if len(parts) > 1 else parts[0]
    return joined, packed, splits, orders


def exchange_and_score(grad_rows, joined, scaling, splits, orders, factors, rows, device_count):
    rank = len(factors)
    middle = list(range(1, rank - 1))
    last = rank - 1
    row_count = grad_rows.shape[0]
    size_last = factors[last][0]
    own = coordinate(lax.axis_index(AXES), factors[last])
    blocks = [joined] + [
        lax.ppermute(joined, AXES, shifted(factors[last], shift, device_count)) for shift in range(1, size_last)
    ]
    full = jnp.concatenate(blocks, axis=0) if size_last > 1 else joined
    total = None
    for (start, size), order in zip(splits, orders):
        prepared = (full[:, start:start + size].astype(jnp.float32) * scaling[start:start + size]).astype(jnp.bfloat16)
        partial = jnp.einsum(
            "rk,qk->rq", grad_rows[:, start:start + size], prepared, preferred_element_type=jnp.float32
        )
        held = list(reversed(order))
        shape = [size_last] + [factors[p][0] for p in held] + [factors[0][0], rows]
        partial = partial.reshape((row_count,) + tuple(shape))
        axes = [0, 1, len(held) + 2] + [held.index(p) + 2 for p in middle] + [len(held) + 3]
        partial = jnp.transpose(partial, axes)
        total = partial if total is None else total + partial
    reverse = jnp.flip(total, axis=1)
    doubled = jnp.concatenate([reverse, reverse], axis=1)
    ordered = lax.dynamic_slice_in_dim(doubled, size_last - 1 - own, size_last, axis=1)
    dims = ordered.ndim
    ordered = jnp.transpose(ordered, [0] + list(range(2, dims - 1)) + [1, dims - 1])
    return ordered.reshape(row_count, -1)


def butterfly_sum(values, factors, device_count):
    for factor in factors:
        size, stride = factor
        bit = 1
        while bit < size:
            pairs = [(i, i + ((coordinate(i, factor) ^ bit) - coordinate(i, factor)) * stride) for i in range(device_count)]
            values = values + lax.ppermute(values, AXES, pairs)
            bit *= 2
    return values


def local(grad_rows, row_weights, destinations, queries, tile_pattern):
    blk_count = lax.axis_size("blk")
    harv_count = lax.axis_size("harvest")
    device_count = blk_count * harv_count
    factors = axis_factors(blk_count, harv_count)
    row_count = grad_rows.shape[0]
    width = grad_rows.shape[1]
    capacity = max(3 * row_count // (2 * blk_count), 2)
    block_size = queries.shape[0] * harv_count
    slot_total = blk_count * capacity
    inv_root = 1.0 / math.sqrt(width)

    query_count = queries.shape[0] * device_count

    squares = jnp.sum(row_weights[:, None] * jnp.square(grad_rows.astype(jnp.float32)), axis=0)
    packed = jnp.concatenate([squares, jnp.zeros((128,), jnp.float32).at[0].set(jnp.sum(row_weights))])
    first = gather_rows(queries, factors[0], device_count)
    first, packed, destinations, tile_pattern = lax.optimization_barrier((first, packed, destinations, tile_pattern))
    joined, packed, splits, orders = gather_streams(first, packed, psum_steps(factors), factors, device_count)
    total_sq, total_weight = packed[:width], packed[width]
    scaling = lax.rsqrt(total_sq / total_weight + 1e-06)
    raw = exchange_and_score(grad_rows, joined, scaling, splits, orders, factors, queries.shape[0], device_count)
    owner_ids = destinations[:, 0]
    pattern_rows = jnp.take(tile_pattern.T, owner_ids, axis=0).astype(jnp.float32)
    full_mask = jnp.repeat(pattern_rows, block_size, axis=1)
    weight_scale = row_weights * inv_root
    value = (raw * weight_scale[:, None] * full_mask).astype(jnp.bfloat16)

    one_hot = (owner_ids[:, None] == jnp.arange(blk_count, dtype=jnp.int32)[None, :]).astype(jnp.int32)
    before = jnp.cumsum(one_hot, axis=0) - one_hot
    slot_rank = jnp.sum(before * one_hot, axis=1)
    slot_index = owner_ids * capacity + slot_rank
    placement = (jnp.arange(slot_total, dtype=jnp.int32)[:, None] == slot_index[None, :]).astype(jnp.bfloat16)
    bucket = jnp.dot(placement, value, preferred_element_type=jnp.float32).astype(jnp.bfloat16)

    received = lax.all_to_all(
        bucket.reshape(blk_count, capacity, query_count), "blk", split_axis=0, concat_axis=0, tiled=True
    )
    return received.reshape(slot_total, query_count)


def solution(mesh):
    in_specs = (
        P(AXES, None),
        P(AXES),
        P(AXES, None),
        P(AXES, None),
        P(),
    )
    out_specs = P(AXES, None)
    return jax.shard_map(local, mesh=mesh, in_specs=in_specs, out_specs=out_specs, check_vma=False)
```

```python
import math

import jax
import jax.numpy as jnp
from jax import lax
from jax.sharding import PartitionSpec as P

AXES = ("blk", "harvest")


def axis_factors(blk_count, harv_count):
    def split(n, lead):
        sizes = []
        if lead and n % 4 == 0:
            sizes.append(4)
            n //= 4
        while n % 2 == 0 and n > 1:
            sizes.append(2)
            n //= 2
        if n > 1:
            sizes.append(n)
        return sizes

    factors = []
    stride = blk_count * harv_count
    for size in split(blk_count, True) + split(harv_count, False):
        stride //= size
        factors.append((size, stride))
    return factors


def coordinate(index, factor):
    size, stride = factor
    return (index // stride) % size


def shifted(factor, shift, device_count):
    size, stride = factor
    return [(i, i + ((coordinate(i, factor) + shift) % size - coordinate(i, factor)) * stride) for i in range(device_count)]


def gather_factor(piece, factor, device_count):
    size, _ = factor
    own = coordinate(lax.axis_index(AXES), factor)
    stacked = jnp.zeros((size,) + piece.shape, piece.dtype)
    stacked = lax.dynamic_update_index_in_dim(stacked, piece, own, 0)
    for shift in range(1, size):
        received = lax.ppermute(piece, AXES, shifted(factor, shift, device_count))
        stacked = lax.dynamic_update_index_in_dim(stacked, received, (own - shift) % size, 0)
    return stacked


def gather_rows(piece, factor, device_count):
    rows = piece.shape[0]
    return gather_factor(piece, factor, device_count).reshape((factor[0] * rows,) + piece.shape[1:])


def column_splits(width, parts):
    blocks = width // 128
    sizes = [(blocks // parts + (1 if j < blocks % parts else 0)) * 128 for j in range(parts)]
    starts = [sum(sizes[:j]) for j in range(parts)]
    return list(zip(starts, sizes))


def psum_steps(factors):
    steps = []
    for factor in factors:
        bit = 1
        while bit < factor[0]:
            steps.append((factor, bit))
            bit *= 2
    return steps


def psum_step(values, step, device_count):
    factor, bit = step
    size, stride = factor
    pairs = [(i, i + ((coordinate(i, factor) ^ bit) - coordinate(i, factor)) * stride) for i in range(device_count)]
    return values + lax.ppermute(values, AXES, pairs)


def gather_streams(first, packed, steps, factors, device_count):
    rank = len(factors)
    middle = list(range(1, rank - 1))
    splits = column_splits(first.shape[1], max(len(middle), 1))
    orders = [middle[j:] + middle[:j] for j in range(len(splits))]
    parts = [first[:, start:start + size] for start, size in splits]
    done = 0
    for level in range(len(middle)):
        parts = [gather_factor(part, factors[order[level]], device_count) for part, order in zip(parts, orders)]
        target = min(level + 2, len(steps) - 1) if level + 1 < len(middle) else len(steps) - 1
        while done < target:
            packed = psum_step(packed, steps[done], device_count)
            done += 1
        if level + 1 < len(middle):
            parts, packed = lax.optimization_barrier((parts, packed))
    parts = [part.reshape(-1, size) for part, (start, size) in zip(parts, splits)]
    joined = jnp.concatenate(parts, axis=1) if len(parts) > 1 else parts[0]
    joined, packed = lax.optimization_barrier((joined, packed))
    while done < len(steps):
        packed = psum_step(packed, steps[done], device_count)
        done += 1
    return joined, packed, splits, orders


def exchange_and_score(grad_rows, joined, scaling, splits, orders, factors, rows, device_count):
    rank = len(factors)
    middle = list(range(1, rank - 1))
    last = rank - 1
    row_count = grad_rows.shape[0]
    size_last = factors[last][0]
    own = coordinate(lax.axis_index(AXES), factors[last])
    blocks = [joined] + [
        lax.ppermute(joined, AXES, shifted(factors[last], shift, device_count)) for shift in range(1, size_last)
    ]
    full = jnp.concatenate(blocks, axis=0) if size_last > 1 else joined
    total = None
    for (start, size), order in zip(splits, orders):
        prepared = (full[:, start:start + size].astype(jnp.float32) * scaling[start:start + size]).astype(jnp.bfloat16)
        partial = jnp.einsum(
            "rk,qk->rq", grad_rows[:, start:start + size], prepared, preferred_element_type=jnp.float32
        )
        held = list(reversed(order))
        shape = [size_last] + [factors[p][0] for p in held] + [factors[0][0], rows]
        partial = partial.reshape((row_count,) + tuple(shape))
        axes = [0, 1, len(held) + 2] + [held.index(p) + 2 for p in middle] + [len(held) + 3]
        partial = jnp.transpose(partial, axes)
        total = partial if total is None else total + partial
    reverse = jnp.flip(total, axis=1)
    doubled = jnp.concatenate([reverse, reverse], axis=1)
    ordered = lax.dynamic_slice_in_dim(doubled, size_last - 1 - own, size_last, axis=1)
    dims = ordered.ndim
    ordered = jnp.transpose(ordered, [0] + list(range(2, dims - 1)) + [1, dims - 1])
    return ordered.reshape(row_count, -1)


def butterfly_sum(values, factors, device_count):
    for factor in factors:
        size, stride = factor
        bit = 1
        while bit < size:
            pairs = [(i, i + ((coordinate(i, factor) ^ bit) - coordinate(i, factor)) * stride) for i in range(device_count)]
            values = values + lax.ppermute(values, AXES, pairs)
            bit *= 2
    return values


def local(grad_rows, row_weights, destinations, queries, tile_pattern):
    blk_count = lax.axis_size("blk")
    harv_count = lax.axis_size("harvest")
    device_count = blk_count * harv_count
    factors = axis_factors(blk_count, harv_count)
    row_count = grad_rows.shape[0]
    width = grad_rows.shape[1]
    capacity = max(3 * row_count // (2 * blk_count), 2)
    block_size = queries.shape[0] * harv_count
    slot_total = blk_count * capacity
    inv_root = 1.0 / math.sqrt(width)

    query_count = queries.shape[0] * device_count

    squares = jnp.sum(row_weights[:, None] * jnp.square(grad_rows.astype(jnp.float32)), axis=0)
    packed = jnp.concatenate([squares, jnp.zeros((128,), jnp.float32).at[0].set(jnp.sum(row_weights))])
    first = gather_rows(queries, factors[0], device_count)
    first, packed, destinations, tile_pattern = lax.optimization_barrier((first, packed, destinations, tile_pattern))
    joined, packed, splits, orders = gather_streams(first, packed, psum_steps(factors), factors, device_count)
    total_sq, total_weight = packed[:width], packed[width]
    scaling = lax.rsqrt(total_sq / total_weight + 1e-06)
    raw = exchange_and_score(grad_rows, joined, scaling, splits, orders, factors, queries.shape[0], device_count)
    owner_ids = destinations[:, 0]
    pattern_rows = jnp.take(tile_pattern.T, owner_ids, axis=0).astype(jnp.float32)
    full_mask = jnp.repeat(pattern_rows, block_size, axis=1)
    weight_scale = row_weights * inv_root
    value = (raw * weight_scale[:, None] * full_mask).astype(jnp.bfloat16)

    one_hot = (owner_ids[:, None] == jnp.arange(blk_count, dtype=jnp.int32)[None, :]).astype(jnp.int32)
    before = jnp.cumsum(one_hot, axis=0) - one_hot
    slot_rank = jnp.sum(before * one_hot, axis=1)
    slot_index = owner_ids * capacity + slot_rank
    placement = (jnp.arange(slot_total, dtype=jnp.int32)[:, None] == slot_index[None, :]).astype(jnp.bfloat16)
    bucket = jnp.dot(placement, value, preferred_element_type=jnp.float32).astype(jnp.bfloat16)

    received = lax.all_to_all(
        bucket.reshape(blk_count, capacity, query_count), "blk", split_axis=0, concat_axis=0, tiled=True
    )
    return received.reshape(slot_total, query_count)


def solution(mesh):
    in_specs = (
        P(AXES, None),
        P(AXES),
        P(AXES, None),
        P(AXES, None),
        P(),
    )
    out_specs = P(AXES, None)
    return jax.shard_map(local, mesh=mesh, in_specs=in_specs, out_specs=out_specs, check_vma=False)
```

```python
import math

import jax
import jax.numpy as jnp
from jax import lax
from jax.sharding import PartitionSpec as P

AXES = ("blk", "harvest")


def axis_factors(blk_count, harv_count):
    def split(n, lead):
        sizes = []
        if lead and n % 4 == 0:
            sizes.append(4)
            n //= 4
        while n % 2 == 0 and n > 1:
            sizes.append(2)
            n //= 2
        if n > 1:
            sizes.append(n)
        return sizes

    factors = []
    stride = blk_count * harv_count
    for size in split(blk_count, True) + split(harv_count, False):
        stride //= size
        factors.append((size, stride))
    return factors


def coordinate(index, factor):
    size, stride = factor
    return (index // stride) % size


def shifted(factor, shift, device_count):
    size, stride = factor
    return [(i, i + ((coordinate(i, factor) + shift) % size - coordinate(i, factor)) * stride) for i in range(device_count)]


def gather_factor(piece, factor, device_count):
    size, _ = factor
    own = coordinate(lax.axis_index(AXES), factor)
    stacked = jnp.zeros((size,) + piece.shape, piece.dtype)
    stacked = lax.dynamic_update_index_in_dim(stacked, piece, own, 0)
    for shift in range(1, size):
        received = lax.ppermute(piece, AXES, shifted(factor, shift, device_count))
        stacked = lax.dynamic_update_index_in_dim(stacked, received, (own - shift) % size, 0)
    return stacked


def gather_rows(piece, factor, device_count):
    rows = piece.shape[0]
    return gather_factor(piece, factor, device_count).reshape((factor[0] * rows,) + piece.shape[1:])


def column_splits(width, parts):
    blocks = width // 128
    sizes = [(blocks // parts + (1 if j < blocks % parts else 0)) * 128 for j in range(parts)]
    starts = [sum(sizes[:j]) for j in range(parts)]
    return list(zip(starts, sizes))


def psum_steps(factors):
    steps = []
    for factor in factors:
        bit = 1
        while bit < factor[0]:
            steps.append((factor, bit))
            bit *= 2
    return steps


def psum_step(values, step, device_count):
    factor, bit = step
    size, stride = factor
    pairs = [(i, i + ((coordinate(i, factor) ^ bit) - coordinate(i, factor)) * stride) for i in range(device_count)]
    return values + lax.ppermute(values, AXES, pairs)


def gather_streams(first, packed, steps, factors, device_count):
    rank = len(factors)
    middle = list(range(1, rank - 1))
    splits = column_splits(first.shape[1], max(len(middle), 1))
    orders = [middle[j:] + middle[:j] for j in range(len(splits))]
    parts = [first[:, start:start + size] for start, size in splits]
    done = 0
    for level in range(len(middle)):
        parts = [gather_factor(part, factors[order[level]], device_count) for part, order in zip(parts, orders)]
        target = min(level + 2, len(steps) - 1) if level + 1 < len(middle) else len(steps) - 1
        while done < target:
            packed = psum_step(packed, steps[done], device_count)
            done += 1
        if level + 1 < len(middle):
            parts, packed = lax.optimization_barrier((parts, packed))
    parts = [part.reshape(-1, size) for part, (start, size) in zip(parts, splits)]
    joined = jnp.concatenate(parts, axis=1) if len(parts) > 1 else parts[0]
    joined, packed = lax.optimization_barrier((joined, packed))
    while done < len(steps):
        packed = psum_step(packed, steps[done], device_count)
        done += 1
    return joined, packed, splits, orders


def exchange_and_score(grad_rows, joined, scaling, splits, orders, factors, rows, device_count):
    rank = len(factors)
    middle = list(range(1, rank - 1))
    last = rank - 1
    row_count = grad_rows.shape[0]
    size_last = factors[last][0]
    own = coordinate(lax.axis_index(AXES), factors[last])
    blocks = [joined] + [
        lax.ppermute(joined, AXES, shifted(factors[last], shift, device_count)) for shift in range(1, size_last)
    ]
    full = jnp.concatenate(blocks, axis=0) if size_last > 1 else joined
    total = None
    for (start, size), order in zip(splits, orders):
        prepared = (full[:, start:start + size].astype(jnp.float32) * scaling[start:start + size]).astype(jnp.bfloat16)
        partial = jnp.einsum(
            "rk,qk->rq", grad_rows[:, start:start + size], prepared, preferred_element_type=jnp.float32
        )
        held = list(reversed(order))
        shape = [size_last] + [factors[p][0] for p in held] + [factors[0][0], rows]
        partial = partial.reshape((row_count,) + tuple(shape))
        axes = [0, 1, len(held) + 2] + [held.index(p) + 2 for p in middle] + [len(held) + 3]
        partial = jnp.transpose(partial, axes)
        total = partial if total is None else total + partial
    reverse = jnp.flip(total, axis=1)
    doubled = jnp.concatenate([reverse, reverse], axis=1)
    ordered = lax.dynamic_slice_in_dim(doubled, size_last - 1 - own, size_last, axis=1)
    dims = ordered.ndim
    ordered = jnp.transpose(ordered, [0] + list(range(2, dims - 1)) + [1, dims - 1])
    return ordered.reshape(row_count, -1)


def butterfly_sum(values, factors, device_count):
    for factor in factors:
        size, stride = factor
        bit = 1
        while bit < size:
            pairs = [(i, i + ((coordinate(i, factor) ^ bit) - coordinate(i, factor)) * stride) for i in range(device_count)]
            values = values + lax.ppermute(values, AXES, pairs)
            bit *= 2
    return values


def local(grad_rows, row_weights, destinations, queries, tile_pattern):
    blk_count = lax.axis_size("blk")
    harv_count = lax.axis_size("harvest")
    device_count = blk_count * harv_count
    factors = axis_factors(blk_count, harv_count)
    row_count = grad_rows.shape[0]
    width = grad_rows.shape[1]
    capacity = max(3 * row_count // (2 * blk_count), 2)
    block_size = queries.shape[0] * harv_count
    slot_total = blk_count * capacity
    inv_root = 1.0 / math.sqrt(width)

    query_count = queries.shape[0] * device_count

    squares = jnp.sum(row_weights[:, None] * jnp.square(grad_rows.astype(jnp.float32)), axis=0)
    packed = jnp.concatenate([squares, jnp.zeros((128,), jnp.float32).at[0].set(jnp.sum(row_weights))])
    first = gather_rows(queries, factors[0], device_count)
    first, packed, destinations, tile_pattern, late_weights = lax.optimization_barrier(
        (first, packed, destinations, tile_pattern, row_weights)
    )
    joined, packed, splits, orders = gather_streams(first, packed, psum_steps(factors), factors, device_count)
    total_sq, total_weight = packed[:width], packed[width]
    scaling = lax.rsqrt(total_sq / total_weight + 1e-06)
    raw = exchange_and_score(grad_rows, joined, scaling, splits, orders, factors, queries.shape[0], device_count)
    owner_ids = destinations[:, 0]
    pattern_rows = jnp.take(tile_pattern.T, owner_ids, axis=0).astype(jnp.float32)
    full_mask = jnp.repeat(pattern_rows, block_size, axis=1)
    weight_scale = late_weights * inv_root
    value = (raw * weight_scale[:, None] * full_mask).astype(jnp.bfloat16)

    one_hot = (owner_ids[:, None] == jnp.arange(blk_count, dtype=jnp.int32)[None, :]).astype(jnp.int32)
    before = jnp.cumsum(one_hot, axis=0) - one_hot
    slot_rank = jnp.sum(before * one_hot, axis=1)
    slot_index = owner_ids * capacity + slot_rank
    placement = (jnp.arange(slot_total, dtype=jnp.int32)[:, None] == slot_index[None, :]).astype(jnp.bfloat16)
    bucket = jnp.dot(placement, value, preferred_element_type=jnp.float32).astype(jnp.bfloat16)

    received = lax.all_to_all(
        bucket.reshape(blk_count, capacity, query_count), "blk", split_axis=0, concat_axis=0, tiled=True
    )
    return received.reshape(slot_total, query_count)


def solution(mesh):
    in_specs = (
        P(AXES, None),
        P(AXES),
        P(AXES, None),
        P(AXES, None),
        P(),
    )
    out_specs = P(AXES, None)
    return jax.shard_map(local, mesh=mesh, in_specs=in_specs, out_specs=out_specs, check_vma=False)
```

```python
import math

import jax
import jax.numpy as jnp
from jax import lax
from jax.sharding import PartitionSpec as P

AXES = ("blk", "harvest")


def axis_factors(blk_count, harv_count):
    def split(n, lead):
        sizes = []
        if lead and n % 4 == 0:
            sizes.append(4)
            n //= 4
        while n % 2 == 0 and n > 1:
            sizes.append(2)
            n //= 2
        if n > 1:
            sizes.append(n)
        return sizes

    factors = []
    stride = blk_count * harv_count
    for size in split(blk_count, True) + split(harv_count, False):
        stride //= size
        factors.append((size, stride))
    return factors


def coordinate(index, factor):
    size, stride = factor
    return (index // stride) % size


def shifted(factor, shift, device_count):
    size, stride = factor
    return [(i, i + ((coordinate(i, factor) + shift) % size - coordinate(i, factor)) * stride) for i in range(device_count)]


def gather_factor(piece, factor, device_count):
    size, _ = factor
    own = coordinate(lax.axis_index(AXES), factor)
    stacked = jnp.zeros((size,) + piece.shape, piece.dtype)
    stacked = lax.dynamic_update_index_in_dim(stacked, piece, own, 0)
    for shift in range(1, size):
        received = lax.ppermute(piece, AXES, shifted(factor, shift, device_count))
        stacked = lax.dynamic_update_index_in_dim(stacked, received, (own - shift) % size, 0)
    return stacked


def gather_rows(piece, factor, device_count):
    rows = piece.shape[0]
    return gather_factor(piece, factor, device_count).reshape((factor[0] * rows,) + piece.shape[1:])


def column_splits(width, parts):
    blocks = width // 128
    sizes = [(blocks // parts + (1 if j < blocks % parts else 0)) * 128 for j in range(parts)]
    starts = [sum(sizes[:j]) for j in range(parts)]
    return list(zip(starts, sizes))


def psum_steps(factors):
    steps = []
    for factor in factors:
        bit = 1
        while bit < factor[0]:
            steps.append((factor, bit))
            bit *= 2
    return steps


def psum_step(values, step, device_count):
    factor, bit = step
    size, stride = factor
    pairs = [(i, i + ((coordinate(i, factor) ^ bit) - coordinate(i, factor)) * stride) for i in range(device_count)]
    return values + lax.ppermute(values, AXES, pairs)


def gather_streams(first, packed, steps, factors, device_count):
    rank = len(factors)
    middle = list(range(1, rank - 1))
    splits = column_splits(first.shape[1], max(len(middle), 1))
    orders = [middle[j:] + middle[:j] for j in range(len(splits))]
    parts = [first[:, start:start + size] for start, size in splits]
    done = 0
    for level in range(len(middle)):
        parts = [gather_factor(part, factors[order[level]], device_count) for part, order in zip(parts, orders)]
        target = min(level + 2, len(steps) - 1) if level + 1 < len(middle) else len(steps) - 1
        while done < target:
            packed = psum_step(packed, steps[done], device_count)
            done += 1
        if level + 1 < len(middle):
            parts, packed = lax.optimization_barrier((parts, packed))
    parts = [part.reshape(-1, size) for part, (start, size) in zip(parts, splits)]
    joined = jnp.concatenate(parts, axis=1) if len(parts) > 1 else parts[0]
    joined, packed = lax.optimization_barrier((joined, packed))
    while done < len(steps):
        packed = psum_step(packed, steps[done], device_count)
        done += 1
    return joined, packed, splits, orders


def exchange_and_score(grad_rows, joined, scaling, splits, orders, factors, rows, device_count):
    rank = len(factors)
    middle = list(range(1, rank - 1))
    last = rank - 1
    row_count = grad_rows.shape[0]
    size_last = factors[last][0]
    own = coordinate(lax.axis_index(AXES), factors[last])
    blocks = [joined] + [
        lax.ppermute(joined, AXES, shifted(factors[last], shift, device_count)) for shift in range(1, size_last)
    ]
    full = jnp.concatenate(blocks, axis=0) if size_last > 1 else joined
    total = None
    for (start, size), order in zip(splits, orders):
        prepared = (full[:, start:start + size].astype(jnp.float32) * scaling[start:start + size]).astype(jnp.bfloat16)
        partial = jnp.einsum(
            "rk,qk->rq", grad_rows[:, start:start + size], prepared, preferred_element_type=jnp.float32
        )
        held = list(reversed(order))
        shape = [size_last] + [factors[p][0] for p in held] + [factors[0][0], rows]
        partial = partial.reshape((row_count,) + tuple(shape))
        axes = [0, 1, len(held) + 2] + [held.index(p) + 2 for p in middle] + [len(held) + 3]
        partial = jnp.transpose(partial, axes)
        total = partial if total is None else total + partial
    reverse = jnp.flip(total, axis=1)
    doubled = jnp.concatenate([reverse, reverse], axis=1)
    ordered = lax.dynamic_slice_in_dim(doubled, size_last - 1 - own, size_last, axis=1)
    dims = ordered.ndim
    ordered = jnp.transpose(ordered, [0] + list(range(2, dims - 1)) + [1, dims - 1])
    return ordered.reshape(row_count, -1)


def butterfly_sum(values, factors, device_count):
    for factor in factors:
        size, stride = factor
        bit = 1
        while bit < size:
            pairs = [(i, i + ((coordinate(i, factor) ^ bit) - coordinate(i, factor)) * stride) for i in range(device_count)]
            values = values + lax.ppermute(values, AXES, pairs)
            bit *= 2
    return values


def local(grad_rows, row_weights, destinations, queries, tile_pattern):
    blk_count = lax.axis_size("blk")
    harv_count = lax.axis_size("harvest")
    device_count = blk_count * harv_count
    factors = axis_factors(blk_count, harv_count)
    row_count = grad_rows.shape[0]
    width = grad_rows.shape[1]
    capacity = max(3 * row_count // (2 * blk_count), 2)
    block_size = queries.shape[0] * harv_count
    slot_total = blk_count * capacity
    inv_root = 1.0 / math.sqrt(width)

    query_count = queries.shape[0] * device_count

    squares = jnp.sum(row_weights[:, None] * jnp.square(grad_rows.astype(jnp.float32)), axis=0)
    packed = jnp.concatenate([squares, jnp.zeros((128,), jnp.float32).at[0].set(jnp.sum(row_weights))])
    first = gather_rows(queries, factors[0], device_count)
    first, packed, destinations, tile_pattern, late_weights = lax.optimization_barrier(
        (first, packed, destinations, tile_pattern, row_weights)
    )
    joined, packed, splits, orders = gather_streams(first, packed, psum_steps(factors), factors, device_count)
    total_sq, total_weight = packed[:width], packed[width]
    scaling = lax.rsqrt(total_sq / total_weight + 1e-06)
    raw = exchange_and_score(grad_rows, joined, scaling, splits, orders, factors, queries.shape[0], device_count)
    owner_ids = destinations[:, 0]
    owner_hot = (owner_ids[:, None] == jnp.arange(blk_count, dtype=jnp.int32)[None, :]).astype(jnp.float32)
    pattern_rows = jnp.dot(owner_hot, tile_pattern.T.astype(jnp.float32), precision=lax.Precision.HIGHEST)
    full_mask = jnp.repeat(pattern_rows, block_size, axis=1)
    weight_scale = late_weights * inv_root
    value = (raw * weight_scale[:, None] * full_mask).astype(jnp.bfloat16)

    earlier = (jnp.arange(row_count)[None, :] < jnp.arange(row_count)[:, None]).astype(jnp.float32)
    before = jnp.dot(earlier, owner_hot, precision=lax.Precision.HIGHEST)
    slot_rank = jnp.sum(before * owner_hot, axis=1).astype(jnp.int32)
    slot_index = owner_ids * capacity + slot_rank
    placement = (jnp.arange(slot_total, dtype=jnp.int32)[:, None] == slot_index[None, :]).astype(jnp.bfloat16)
    bucket = jnp.dot(placement, value, preferred_element_type=jnp.float32).astype(jnp.bfloat16)

    received = lax.all_to_all(
        bucket.reshape(blk_count, capacity, query_count), "blk", split_axis=0, concat_axis=0, tiled=True
    )
    return received.reshape(slot_total, query_count)


def solution(mesh):
    in_specs = (
        P(AXES, None),
        P(AXES),
        P(AXES, None),
        P(AXES, None),
        P(),
    )
    out_specs = P(AXES, None)
    return jax.shard_map(local, mesh=mesh, in_specs=in_specs, out_specs=out_specs, check_vma=False)
```
